512 devices in a mesh: section: 8 (over y), expert: 32 (over z, x_hi, core), dp: 2 (over x_lo).
Axes of the slice: x: 4 (x_hi: 2, x_lo: 2; x = x_hi * 2 + x_lo), y: 8, z: 8, core: 2. Of those that a mesh axis runs over, the one named last changes fastest.
Arguments:
- blocks: bfloat16 [8, 512, 7168], P('section', ('expert', 'dp')), may hold values from -6 to 6
- gains: float32 [8, 7168], P('section'), may hold values from 0.1 to 1.9
- w_gate: bfloat16 [8, 7168, 4096], P('section', 'dp', 'expert'), may hold values from -0.0625 to 0.0625
- w_up: bfloat16 [8, 7168, 4096], P('section', 'dp', 'expert'), may hold values from -0.0625 to 0.0625
- w_down: bfloat16 [8, 7168, 4096], P('section', 'dp', 'expert'), may hold values from -0.1875 to 0.1875
- expert_ids: int32 [8, 2, 512, 2], P('section', None, ('expert', 'dp')), may hold values from 0 to 3, all different within a row; in each aligned block of 8 rows (0 to 7, 8 to 15, ..., all dimensions but the last counted through in order) at most 5 rows name the same one
- combine: float32 [8, 2, 512, 2], P('section', None, ('expert', 'dp')), may hold values from 0.2 to 1
Outputs:
- finished: bfloat16 [8, 512, 7168], P('section', ('expert', 'dp'))
The draws below stay inside these ranges and needn't reach their ends.
Inputs may be any that keep to these rules, and one draw needn't show every extreme that they name: `expert_ids`: each token names 2 different experts; within the 8 tokens of one device (aligned blocks), no expert is named more than 5 times, a bound that some block reaches.
All inputs are finite; a program needn't handle non-finite values.
Results may differ from the reference program's by a relative error of at most 0.0073.
Values may be sent and summed in bfloat16 or wider, within the bound.
No kernel may reach another device: no remote copies, remote signals or barrier semaphores. Data moves between devices by JAX's collectives and lax.ppermute only.
A program may use at most 64 MiB of HBM per device.

```python
import math
import jax
import jax.numpy as jnp
import numpy as np
from jax import lax

D = 7168
FF = 1024
TOP = 2
ROUNDS = 2
TOK_DEV = 8
EXPERTS = 4
CAP = 5
TOKENS = 512
N_SECTION = 8
N_EXPERT = 32


def level_of(own_key, dims, cuts, low, high):
    def one(position, parts):
        heights = jax.random.uniform(jax.random.fold_in(jax.random.fold_in(own_key, 6), position), (parts,), jnp.float32, low / len(cuts), high / len(cuts))
        return jnp.repeat(jnp.exp(heights), dims[position] // parts).reshape((-1,) + (1,) * (len(dims) - position - 1))

    level = one(*cuts[0])
    for cut in cuts[1:]:
        level = level * one(*cut)
    return level


def assign_block(rng, own, number, rows, amount, top, reach, slope):
    sequence = jax.random.permutation(rng, amount)
    crowded, common = load_shares(amount, rows * top, reach, slope, True), load_shares(amount, rows * top, reach, slope, False)
    places = jnp.arange(amount)

    def named(sizes, rotation):
        used = int((sizes > 0).sum())
        fixed = max(1, used // 4)
        shifted = fixed + (places - fixed + rotation * (used - fixed)) % max(1, amount - fixed)
        return jnp.zeros((amount,), jnp.int32).at[sequence[jnp.where(places < fixed, places, shifted)]].set(jnp.asarray(sizes, jnp.int32))

    sizes = jnp.where(number % 4 == 0, named(crowded, number // 4), named(common, number - number // 4 - 1))
    mixed = jax.random.permutation(jax.random.fold_in(own, 3), amount)
    giver, sink = mixed[0:amount // 2 * 2:2], mixed[1:amount // 2 * 2:2]
    slack = jnp.minimum(sizes[giver] - 1, reach - sizes[sink]) // 2
    slack = jnp.where((giver == sequence[0]) | (sink == sequence[0]) | (sizes[sink] == 0), 0, jnp.maximum(slack, 0))
    shifted = jax.random.randint(jax.random.fold_in(own, 4), (amount // 2,), 0, 1 << 20) % (slack + 1)
    sizes = sizes.at[giver].add(-shifted).at[sink].add(shifted)
    items = jnp.searchsorted(jnp.cumsum(sizes), jnp.arange(rows * top), side="right").astype(jnp.int32)
    grid = items.reshape(top, rows).T
    grid = grid[jax.random.permutation(jax.random.fold_in(own, 1), rows)]
    rotation = jax.random.randint(jax.random.fold_in(own, 2), (rows, 1), 0, top)
    return jnp.take_along_axis(grid, (jnp.arange(top)[None, :] + rotation) % top, axis=1)


def load_shares(count, total, bound, slope, full):
    portions = [(1 << 20) // math.isqrt(standing ** slope) + 1 for standing in range(1, count + 1)]
    largest = bound if full else min(bound, max(-(-total // count), total * portions[0] // sum(portions)))
    least = 1 if total - largest >= count - 1 else 0
    counts, surplus = [largest] + [least] * (count - 1), total - largest - least * (count - 1)
    while surplus > 0:
        candidates = [i for i in range(1, count) if counts[i] < largest] or [i for i in range(1, count) if counts[i] < bound]
        pool, budget = sum([portions[i] for i in candidates]), surplus
        for i in candidates:
            more = min(bound - counts[i], max(1, budget * portions[i] // pool), surplus)
            counts[i] = counts[i] + more
            surplus = surplus - more
    return np.array(counts)


def bell_draw(rng, dims, deviation, reach, split=(), held_as=jnp.bfloat16):
    result = jax.random.normal(rng, dims, jnp.float32) * deviation
    if len(split) > 0:
        result = level_of(rng, dims, split, -0.22, 0.18) * result
    return jnp.clip(result, min=-reach, max=reach).astype(held_as)


def setup_inputs(seed: int = 0) -> dict:
    key_of = jax.random.split(jax.random.key(seed), 8)
    blocks = bell_draw(key_of[0], (N_SECTION, TOKENS, D), 1.0, 6.0, ((0, 8), (1, 64)))
    gains = jnp.clip(1.0 + 0.18 * jax.random.normal(key_of[1], (N_SECTION, D), jnp.float32), 0.1, 1.9)
    w_gate = bell_draw(key_of[2], (N_SECTION, D, EXPERTS * FF), D ** -0.5, 0.0625, ((0, 8), (1, 2), (2, 32)))
    w_up = bell_draw(key_of[3], (N_SECTION, D, EXPERTS * FF), D ** -0.5, 0.0625, ((0, 8), (1, 2), (2, 32)))
    w_down = bell_draw(key_of[4], (N_SECTION, D, EXPERTS * FF), FF ** -0.5, 0.1875, ((0, 8), (1, 2), (2, 32)))
    expert_ids_keys = jax.random.split(jax.random.fold_in(key_of[5], 1), N_SECTION * ROUNDS * TOKENS // TOK_DEV)
    expert_ids_turns = jax.random.permutation(jax.random.fold_in(key_of[5], 3), N_SECTION * ROUNDS * TOKENS // TOK_DEV)
    expert_ids = jax.vmap(lambda own, number: assign_block(jax.random.fold_in(key_of[5], 2), own, number, TOK_DEV, EXPERTS, TOP, CAP, 2))(expert_ids_keys, expert_ids_turns).reshape((N_SECTION, ROUNDS, TOKENS, TOP))
    combine = jnp.clip(0.2 + 0.8 * jax.random.uniform(key_of[6], (N_SECTION, ROUNDS, TOKENS, TOP), jnp.float32) ** level_of(key_of[6], (N_SECTION, ROUNDS, TOKENS, TOP), ((0, 8), (2, 64)), -0.2, 0.2), 0.2, 1.0)
    return dict(blocks=blocks, gains=gains, w_gate=w_gate, w_up=w_up, w_down=w_down, expert_ids=expert_ids, combine=combine)


def layer_step(stream, gain_row, gate_w, up_w, down_w, route, mixing):
    widened = stream.astype(jnp.float32)
    inv_rms = lax.rsqrt(lax.optimization_barrier(jnp.mean(widened * widened, axis=1, keepdims=True)) + 1e-06)
    normed = (widened * inv_rms * gain_row[None, :]).astype(jnp.bfloat16)
    sources = TOKENS // TOK_DEV
    span = N_EXPERT // EXPERTS
    slice_width = FF // span
    grouped = route.reshape(sources, TOK_DEV * TOP)
    chosen = (grouped[:, :, None] == jnp.arange(EXPERTS, dtype=jnp.int32)[None, None, :]).astype(jnp.int32)
    running = jnp.cumsum(chosen, axis=1)
    slot_of = lax.optimization_barrier(jnp.sum(chosen * (running - 1), axis=2)).astype(jnp.int32)
    row_of = (jnp.arange(sources, dtype=jnp.int32)[:, None] * CAP + slot_of).reshape(-1).astype(jnp.int32)
    flat_ids = route.reshape(-1).astype(jnp.int32)
    copies = jnp.repeat(normed, TOP, axis=0)
    buffer = jnp.zeros((EXPERTS, sources * CAP, D), jnp.bfloat16).at[flat_ids, row_of].set(copies)
    gate_each = gate_w.reshape(D, EXPERTS, FF).transpose(1, 0, 2)
    up_each = up_w.reshape(D, EXPERTS, FF).transpose(1, 0, 2)
    down_each = down_w.reshape(D, EXPERTS, FF).transpose(1, 0, 2)

    def one_expert(operands):
        rows_in, gate_full, up_full, down_full = operands
        gate_act = jnp.dot(rows_in, gate_full, preferred_element_type=jnp.float32)
        upward = jnp.dot(rows_in, up_full, preferred_element_type=jnp.float32)
        hidden = (jax.nn.silu(gate_act) * upward).astype(jnp.bfloat16)
        hidden_blocks = hidden.astype(jnp.float32).reshape(rows_in.shape[0], span, slice_width)
        down_blocks = down_full.astype(jnp.float32).reshape(D, span, slice_width)
        pieces = jnp.einsum('rsf,dsf->srd', hidden_blocks, down_blocks)
        rounded = lax.optimization_barrier(pieces.astype(jnp.bfloat16))
        return lax.optimization_barrier(jnp.sum(rounded.astype(jnp.float32), axis=0)).astype(jnp.bfloat16)
    outputs = lax.map(one_expert, (buffer, gate_each, up_each, down_each))
    picked = outputs[flat_ids, row_of].reshape(TOKENS, TOP, D)
    mixed_sum = lax.optimization_barrier(jnp.sum(mixing[:, :, None] * picked.astype(jnp.float32), axis=1))
    return (widened + mixed_sum).astype(jnp.bfloat16)

def reference(blocks, gains, w_gate, w_up, w_down, expert_ids, combine):
    finished = []
    for section_pos in range(N_SECTION):
        start_block = (section_pos - ROUNDS + 1) % N_SECTION
        stream = blocks[start_block]
        for layer_turn in range(ROUNDS):
            layer_index = (start_block + layer_turn) % N_SECTION
            stream = layer_step(stream, gains[layer_index], w_gate[layer_index], w_up[layer_index], w_down[layer_index], expert_ids[layer_index, layer_turn], combine[layer_index, layer_turn])
        finished.append(stream)
    return jnp.stack(finished)
```

```python
from functools import partial

import jax
import jax.numpy as jnp
import numpy as np
from jax import lax
from jax.sharding import Mesh
from jax.sharding import PartitionSpec as P

ALL = ("eg", "q", "dp")


def passed_along(array, axis, by):
    length = lax.axis_size(axis)
    return lax.ppermute(array, axis, [(i, (i + by) % length) for i in range(length)])


def route(stream, gain_row, routes, experts, capacity):
    tok_rows, model_width = stream.shape
    fan_out = routes.shape[1]
    widened = stream.astype(jnp.float32)
    inv_rms = lax.rsqrt(jnp.mean(widened * widened, axis=1, keepdims=True) + 1e-06)
    normed = (widened * inv_rms * gain_row[None, :]).astype(jnp.bfloat16)
    flat_ids = routes.reshape(-1)
    count_all = flat_ids.shape[0]
    chosen = (flat_ids[:, None] == jnp.arange(experts, dtype=jnp.int32)[None, :]).astype(
        jnp.float32
    )
    triangle = (jnp.arange(count_all)[:, None] >= jnp.arange(count_all)[None, :]).astype(
        jnp.float32
    )
    running = jnp.dot(triangle, chosen, preferred_element_type=jnp.float32)
    slot_of = jnp.sum(chosen * (running - 1.0), axis=1).astype(jnp.int32)
    target = flat_ids * capacity + slot_of
    placing = jnp.arange(experts * capacity, dtype=jnp.int32)[:, None] == target[None, :]
    placing = (
        placing.reshape(experts * capacity, tok_rows, fan_out).any(axis=2).astype(jnp.bfloat16)
    )
    outgoing = jnp.dot(placing, normed, preferred_element_type=jnp.float32).astype(jnp.bfloat16)
    return widened, outgoing.reshape(experts, capacity, model_width), target


def moe_layer(stream, gain_row, gate_w, up_w, down_mine, routes, mixing):
    experts = lax.axis_size("eg")
    blocks = lax.axis_size("q")
    halves = lax.axis_size("dp")
    tok_rows, model_width = stream.shape
    fan_out = routes.shape[1]
    capacity = min(tok_rows, max(2, 5 * tok_rows * fan_out // (4 * experts)))
    half = model_width // halves
    widened, outgoing, target = route(stream, gain_row, routes, experts, capacity)
    send = outgoing.reshape(experts, 1, capacity, halves, half).transpose(0, 1, 3, 2, 4)
    send = jnp.broadcast_to(send, (experts, blocks, halves, capacity, half))
    send = send.reshape(experts * blocks * halves, capacity, half)
    arrived = lax.all_to_all(send, ALL, split_axis=0, concat_axis=0, tiled=True)
    sources = arrived.shape[0]
    rows = arrived.reshape(sources * capacity, half)
    gate_part = jnp.dot(rows, gate_w, preferred_element_type=jnp.float32)
    up_part = jnp.dot(rows, up_w, preferred_element_type=jnp.float32)
    both = lax.psum(jnp.stack([gate_part, up_part]), "dp")
    hidden = (jax.nn.silu(both[0]) * both[1]).astype(jnp.bfloat16)
    hidden_all = lax.all_gather(hidden, "q", axis=1, tiled=True)
    out = lax.dot_general(
        hidden_all, down_mine, (((1,), (1,)), ((), ())), preferred_element_type=jnp.float32
    ).astype(jnp.bfloat16)
    piece = out.shape[1]
    back = lax.all_to_all(
        out.reshape(sources, capacity, piece), ALL, split_axis=0, concat_axis=0, tiled=True
    )
    back = back.reshape(experts, blocks, halves, capacity, piece).transpose(0, 3, 2, 1, 4)
    expert_out = back.reshape(experts * capacity, model_width)
    picked = jnp.take(expert_out, target, axis=0)
    picked = picked.reshape(tok_rows, fan_out, model_width)
    mixed_sum = jnp.sum(mixing[:, :, None] * picked.astype(jnp.float32), axis=1)
    return (widened + mixed_sum).astype(jnp.bfloat16)


def on_device(blocks, gains, w_gate, w_up, w_down, expert_ids, combine):
    stream = blocks[0]
    turns = expert_ids.shape[1]
    n_blocks = lax.axis_size("q")
    down_local = w_down[0]
    half, width = down_local.shape
    piece = half // n_blocks
    down_mine = lax.all_to_all(
        down_local.reshape(n_blocks, piece, width), "q", split_axis=0, concat_axis=0, tiled=True
    )
    down_mine = down_mine.transpose(1, 0, 2).reshape(piece, n_blocks * width)
    for layer_turn in range(turns):
        if layer_turn > 0:
            stream = passed_along(stream, "section", 1)
        stream = moe_layer(
            stream,
            gains[0],
            w_gate[0],
            w_up[0],
            down_mine,
            expert_ids[0, layer_turn],
            combine[0, layer_turn],
        )
    return stream[None]


def solution(mesh):
    n_section, n_expert, n_dp = (mesh.shape[a] for a in ("section", "expert", "dp"))
    n_q = n_expert // 4
    inner = Mesh(
        np.asarray(mesh.devices).reshape(n_section, n_expert // n_q, n_q, n_dp),
        ("section", "eg", "q", "dp"),
    )
    tok = ("eg", "q", "dp")
    in_specs = (
        P("section", tok, None),
        P("section", None),
        P("section", "dp", ("eg", "q")),
        P("section", "dp", ("eg", "q")),
        P("section", "dp", ("eg", "q")),
        P("section", None, tok, None),
        P("section", None, tok, None),
    )
    out_specs = P("section", tok, None)
    return jax.shard_map(
        on_device, mesh=inner, in_specs=in_specs, out_specs=out_specs, check_vma=False
    )
```

```python
from functools import partial

import jax
import jax.numpy as jnp
import numpy as np
from jax import lax
from jax.sharding import Mesh
from jax.sharding import PartitionSpec as P

ALL = ("eg", "q", "dp")


def passed_along(array, axis, by):
    length = lax.axis_size(axis)
    return lax.ppermute(array, axis, [(i, (i + by) % length) for i in range(length)])


def route(stream, gain_row, routes, experts, capacity):
    tok_rows, model_width = stream.shape
    fan_out = routes.shape[1]
    widened = stream.astype(jnp.float32)
    inv_rms = lax.rsqrt(jnp.mean(widened * widened, axis=1, keepdims=True) + 1e-06)
    normed = (widened * inv_rms * gain_row[None, :]).astype(jnp.bfloat16)
    flat_ids = routes.reshape(-1)
    count_all = flat_ids.shape[0]
    chosen = (flat_ids[:, None] == jnp.arange(experts, dtype=jnp.int32)[None, :]).astype(
        jnp.float32
    )
    triangle = (jnp.arange(count_all)[:, None] >= jnp.arange(count_all)[None, :]).astype(
        jnp.float32
    )
    running = jnp.dot(triangle, chosen, preferred_element_type=jnp.float32)
    slot_of = jnp.sum(chosen * (running - 1.0), axis=1).astype(jnp.int32)
    target = flat_ids * capacity + slot_of
    placing = jnp.arange(experts * capacity, dtype=jnp.int32)[:, None] == target[None, :]
    placing = (
        placing.reshape(experts * capacity, tok_rows, fan_out).any(axis=2).astype(jnp.bfloat16)
    )
    outgoing = jnp.dot(placing, normed, preferred_element_type=jnp.float32).astype(jnp.bfloat16)
    return widened, outgoing.reshape(experts, capacity, model_width), target


def moe_layer(stream, gain_row, gate_w, up_w, down_mine, routes, mixing):
    experts = lax.axis_size("eg")
    blocks = lax.axis_size("q")
    halves = lax.axis_size("dp")
    tok_rows, model_width = stream.shape
    fan_out = routes.shape[1]
    capacity = min(tok_rows, max(2, 5 * tok_rows * fan_out // (4 * experts)))
    half = model_width // halves
    widened, outgoing, target = route(stream, gain_row, routes, experts, capacity)
    send = outgoing.reshape(experts, capacity, halves, half).transpose(0, 2, 1, 3)
    send = send.reshape(experts * halves, capacity, half)
    arrived = lax.all_to_all(send, ("eg", "dp"), split_axis=0, concat_axis=0, tiled=True)
    arrived = lax.all_gather(arrived, "q", axis=0, tiled=False)
    sources = blocks * experts * halves
    rows = arrived.reshape(sources * capacity, half)
    gate_part = jnp.dot(rows, gate_w, preferred_element_type=jnp.float32)
    up_part = jnp.dot(rows, up_w, preferred_element_type=jnp.float32)
    mine = jnp.stack([gate_part, up_part])
    both = mine + passed_along(mine, "dp", 1)
    hidden = (jax.nn.silu(both[0]) * both[1]).astype(jnp.bfloat16)
    hidden_all = lax.all_gather(hidden, "q", axis=1, tiled=True)
    out = lax.dot_general(
        hidden_all, down_mine, (((1,), (1,)), ((), ())), preferred_element_type=jnp.float32
    ).astype(jnp.bfloat16)
    piece = out.shape[1]
    out = out.reshape(blocks, experts, halves, capacity, piece).transpose(1, 0, 2, 3, 4)
    back = lax.all_to_all(
        out.reshape(sources, capacity, piece), ALL, split_axis=0, concat_axis=0, tiled=True
    )
    back = back.reshape(experts, blocks, halves, capacity, piece).transpose(0, 3, 2, 1, 4)
    expert_out = back.reshape(experts * capacity, model_width)
    picked = jnp.take(expert_out, target, axis=0)
    picked = picked.reshape(tok_rows, fan_out, model_width)
    mixed_sum = jnp.sum(mixing[:, :, None] * picked.astype(jnp.float32), axis=1)
    return (widened + mixed_sum).astype(jnp.bfloat16)


def on_device(blocks, gains, w_gate, w_up, w_down, expert_ids, combine):
    stream = blocks[0]
    turns = expert_ids.shape[1]
    n_blocks = lax.axis_size("q")
    down_local = w_down[0]
    half, width = down_local.shape
    piece = half // n_blocks
    down_mine = lax.all_to_all(
        down_local.reshape(n_blocks, piece, width), "q", split_axis=0, concat_axis=0, tiled=True
    )
    down_mine = down_mine.transpose(1, 0, 2).reshape(piece, n_blocks * width)
    for layer_turn in range(turns):
        if layer_turn > 0:
            stream = passed_along(stream, "section", 1)
        stream = moe_layer(
            stream,
            gains[0],
            w_gate[0],
            w_up[0],
            down_mine,
            expert_ids[0, layer_turn],
            combine[0, layer_turn],
        )
    return stream[None]


def solution(mesh):
    n_section, n_expert, n_dp = (mesh.shape[a] for a in ("section", "expert", "dp"))
    n_q = n_expert // 4
    inner = Mesh(
        np.asarray(mesh.devices).reshape(n_section, n_expert // n_q, n_q, n_dp),
        ("section", "eg", "q", "dp"),
    )
    tok = ("eg", "q", "dp")
    in_specs = (
        P("section", tok, None),
        P("section", None),
        P("section", "dp", ("eg", "q")),
        P("section", "dp", ("eg", "q")),
        P("section", "dp", ("eg", "q")),
        P("section", None, tok, None),
        P("section", None, tok, None),
    )
    out_specs = P("section", tok, None)
    return jax.shard_map(
        on_device, mesh=inner, in_specs=in_specs, out_specs=out_specs, check_vma=False
    )
```

```python
from functools import partial

import jax
import jax.numpy as jnp
import numpy as np
from jax import lax
from jax.sharding import Mesh
from jax.sharding import PartitionSpec as P

ALL = ("eg", "q", "dp")


def passed_along(array, axis, by):
    length = lax.axis_size(axis)
    return lax.ppermute(array, axis, [(i, (i + by) % length) for i in range(length)])


def route(stream, gain_row, routes, experts, capacity):
    tok_rows, model_width = stream.shape
    fan_out = routes.shape[1]
    widened = stream.astype(jnp.float32)
    inv_rms = lax.rsqrt(jnp.mean(widened * widened, axis=1, keepdims=True) + 1e-06)
    normed = (widened * inv_rms * gain_row[None, :]).astype(jnp.bfloat16)
    flat_ids = routes.reshape(-1)
    count_all = flat_ids.shape[0]
    chosen = (flat_ids[:, None] == jnp.arange(experts, dtype=jnp.int32)[None, :]).astype(
        jnp.float32
    )
    triangle = (jnp.arange(count_all)[:, None] >= jnp.arange(count_all)[None, :]).astype(
        jnp.float32
    )
    running = jnp.dot(triangle, chosen, preferred_element_type=jnp.float32)
    slot_of = jnp.sum(chosen * (running - 1.0), axis=1).astype(jnp.int32)
    target = flat_ids * capacity + slot_of
    placing = jnp.arange(experts * capacity, dtype=jnp.int32)[:, None] == target[None, :]
    placing = (
        placing.reshape(experts * capacity, tok_rows, fan_out).any(axis=2).astype(jnp.bfloat16)
    )
    outgoing = jnp.dot(placing, normed, preferred_element_type=jnp.float32).astype(jnp.bfloat16)
    return widened, outgoing.reshape(experts, capacity, model_width), target


def moe_layer(stream, gain_row, gate_w, up_w, down_mine, routes, mixing):
    experts = lax.axis_size("eg")
    blocks = lax.axis_size("q")
    halves = lax.axis_size("dp")
    tok_rows, model_width = stream.shape
    fan_out = routes.shape[1]
    capacity = min(tok_rows, max(2, 5 * tok_rows * fan_out // (4 * experts)))
    half = model_width // halves
    widened, outgoing, target = route(stream, gain_row, routes, experts, capacity)
    lanes = 128
    tiles = half // lanes
    send = outgoing.reshape(experts, capacity, halves, tiles, lanes).transpose(0, 2, 1, 3, 4)
    send = send.reshape(experts * halves, capacity * tiles, lanes)
    arrived = lax.all_to_all(send, ("eg", "dp"), split_axis=0, concat_axis=0, tiled=True)
    arrived = arrived.reshape(experts * halves, capacity, half).transpose(1, 0, 2)
    arrived = lax.all_gather(arrived, "q", axis=1, tiled=True)
    sources = blocks * experts * halves
    rows = arrived.reshape(capacity * sources, half)
    gate_part = jnp.dot(rows, gate_w, preferred_element_type=jnp.float32)
    up_part = jnp.dot(rows, up_w, preferred_element_type=jnp.float32)
    mine = jnp.stack([gate_part, up_part])
    both = mine + passed_along(mine, "dp", 1)
    hidden = (jax.nn.silu(both[0]) * both[1]).astype(jnp.bfloat16)
    hidden_all = lax.all_gather(hidden, "q", axis=1, tiled=True)
    out = lax.dot_general(
        hidden_all, down_mine, (((1,), (1,)), ((), ())), preferred_element_type=jnp.float32
    ).astype(jnp.bfloat16)
    piece = out.shape[1]
    out = out.reshape(capacity, blocks, experts, halves, piece).transpose(2, 1, 3, 0, 4)
    back = lax.all_to_all(
        out.reshape(sources, capacity, piece), ALL, split_axis=0, concat_axis=0, tiled=True
    )
    back = back.reshape(experts, blocks, halves, capacity, piece).transpose(0, 3, 2, 1, 4)
    expert_out = back.reshape(experts * capacity, model_width)
    picked = jnp.take(expert_out, target, axis=0)
    picked = picked.reshape(tok_rows, fan_out, model_width)
    mixed_sum = jnp.sum(mixing[:, :, None] * picked.astype(jnp.float32), axis=1)
    return (widened + mixed_sum).astype(jnp.bfloat16)


def on_device(blocks, gains, w_gate, w_up, w_down, expert_ids, combine):
    stream = blocks[0]
    turns = expert_ids.shape[1]
    n_blocks = lax.axis_size("q")
    down_local = w_down[0]
    half, width = down_local.shape
    piece = half // n_blocks
    down_mine = lax.all_to_all(
        down_local.reshape(n_blocks, piece, width), "q", split_axis=0, concat_axis=0, tiled=True
    )
    down_mine = down_mine.transpose(1, 0, 2).reshape(piece, n_blocks * width)
    for layer_turn in range(turns):
        if layer_turn > 0:
            stream = passed_along(stream, "section", 1)
        stream = moe_layer(
            stream,
            gains[0],
            w_gate[0],
            w_up[0],
            down_mine,
            expert_ids[0, layer_turn],
            combine[0, layer_turn],
        )
    return stream[None]


def solution(mesh):
    n_section, n_expert, n_dp = (mesh.shape[a] for a in ("section", "expert", "dp"))
    n_q = n_expert // 4
    inner = Mesh(
        np.asarray(mesh.devices).reshape(n_section, n_expert // n_q, n_q, n_dp),
        ("section", "eg", "q", "dp"),
    )
    tok = ("eg", "q", "dp")
    in_specs = (
        P("section", tok, None),
        P("section", None),
        P("section", "dp", ("eg", "q")),
        P("section", "dp", ("eg", "q")),
        P("section", "dp", ("eg", "q")),
        P("section", None, tok, None),
        P("section", None, tok, None),
    )
    out_specs = P("section", tok, None)
    return jax.shard_map(
        on_device, mesh=inner, in_specs=in_specs, out_specs=out_specs, check_vma=False
    )
```

```python
from functools import partial

import jax
import jax.numpy as jnp
import numpy as np
from jax import lax
from jax.sharding import Mesh
from jax.sharding import PartitionSpec as P

ALL = ("eg", "q", "dp")


def passed_along(array, axis, by):
    length = lax.axis_size(axis)
    return lax.ppermute(array, axis, [(i, (i + by) % length) for i in range(length)])


def route(stream, gain_row, routes, experts, capacity):
    tok_rows, model_width = stream.shape
    fan_out = routes.shape[1]
    widened = stream.astype(jnp.float32)
    inv_rms = lax.rsqrt(jnp.mean(widened * widened, axis=1, keepdims=True) + 1e-06)
    normed = (widened * inv_rms * gain_row[None, :]).astype(jnp.bfloat16)
    flat_ids = routes.reshape(-1)
    count_all = flat_ids.shape[0]
    chosen = (flat_ids[:, None] == jnp.arange(experts, dtype=jnp.int32)[None, :]).astype(
        jnp.float32
    )
    triangle = (jnp.arange(count_all)[:, None] >= jnp.arange(count_all)[None, :]).astype(
        jnp.float32
    )
    running = jnp.dot(triangle, chosen, preferred_element_type=jnp.float32)
    slot_of = jnp.sum(chosen * (running - 1.0), axis=1).astype(jnp.int32)
    target = flat_ids * capacity + slot_of
    placing = jnp.arange(experts * capacity, dtype=jnp.int32)[:, None] == target[None, :]
    placing = (
        placing.reshape(experts * capacity, tok_rows, fan_out).any(axis=2).astype(jnp.bfloat16)
    )
    outgoing = jnp.dot(placing, normed, preferred_element_type=jnp.float32).astype(jnp.bfloat16)
    return widened, outgoing.reshape(experts, capacity, model_width), target


def moe_layer(stream, gain_row, gate_w, up_w, down_mine, routes, mixing):
    experts = lax.axis_size("eg")
    blocks = lax.axis_size("q")
    halves = lax.axis_size("dp")
    tok_rows, model_width = stream.shape
    fan_out = routes.shape[1]
    capacity = min(tok_rows, max(2, 5 * tok_rows * fan_out // (4 * experts)))
    half = model_width // halves
    widened, outgoing, target = route(stream, gain_row, routes, experts, capacity)
    lanes = 128
    tiles = half // lanes
    send = outgoing.reshape(experts, capacity, halves, tiles, lanes).transpose(0, 2, 1, 3, 4)
    send = send.reshape(experts * halves, capacity * tiles, lanes)
    arrived = lax.all_to_all(send, ("eg", "dp"), split_axis=0, concat_axis=0, tiled=True)
    arrived = arrived.reshape(experts * halves, capacity, half).transpose(1, 0, 2)
    arrived = lax.all_gather(arrived, "q", axis=1, tiled=True)
    sources = blocks * experts * halves
    rows = arrived.reshape(capacity * sources, half)
    gate_part = jnp.dot(rows, gate_w, preferred_element_type=jnp.float32)
    up_part = jnp.dot(rows, up_w, preferred_element_type=jnp.float32)
    mine = jnp.stack([gate_part, up_part])
    both = mine + passed_along(mine, "dp", 1)
    hidden = (jax.nn.silu(both[0]) * both[1]).astype(jnp.bfloat16)
    hidden_all = lax.all_gather(hidden, "q", axis=1, tiled=True)
    out = lax.dot_general(
        hidden_all, down_mine, (((1,), (1,)), ((), ())), preferred_element_type=jnp.float32
    ).astype(jnp.bfloat16)
    piece = out.shape[1]
    out = out.reshape(capacity, blocks, experts, halves, piece).transpose(2, 1, 3, 0, 4)
    back = lax.all_to_all(
        out.reshape(sources, capacity * piece), ALL, split_axis=0, concat_axis=0, tiled=True
    )
    back = back.reshape(experts, blocks, halves, capacity, piece).transpose(0, 3, 2, 1, 4)
    expert_out = back.reshape(experts * capacity, model_width)
    picked = jnp.take(expert_out, target, axis=0)
    picked = picked.reshape(tok_rows, fan_out, model_width)
    mixed_sum = jnp.sum(mixing[:, :, None] * picked.astype(jnp.float32), axis=1)
    return (widened + mixed_sum).astype(jnp.bfloat16)


def on_device(blocks, gains, w_gate, w_up, w_down, expert_ids, combine):
    stream = blocks[0]
    turns = expert_ids.shape[1]
    n_blocks = lax.axis_size("q")
    down_local = w_down[0]
    half, width = down_local.shape
    piece = half // n_blocks
    down_mine = lax.all_to_all(
        down_local.reshape(n_blocks, piece, width), "q", split_axis=0, concat_axis=0, tiled=True
    )
    down_mine = down_mine.transpose(1, 0, 2).reshape(piece, n_blocks * width)
    for layer_turn in range(turns):
        if layer_turn > 0:
            stream = passed_along(stream, "section", 1)
        stream = moe_layer(
            stream,
            gains[0],
            w_gate[0],
            w_up[0],
            down_mine,
            expert_ids[0, layer_turn],
            combine[0, layer_turn],
        )
    return stream[None]


def solution(mesh):
    n_section, n_expert, n_dp = (mesh.shape[a] for a in ("section", "expert", "dp"))
    n_q = n_expert // 4
    inner = Mesh(
        np.asarray(mesh.devices).reshape(n_section, n_expert // n_q, n_q, n_dp),
        ("section", "eg", "q", "dp"),
    )
    tok = ("eg", "q", "dp")
    in_specs = (
        P("section", tok, None),
        P("section", None),
        P("section", "dp", ("eg", "q")),
        P("section", "dp", ("eg", "q")),
        P("section", "dp", ("eg", "q")),
        P("section", None, tok, None),
        P("section", None, tok, None),
    )
    out_specs = P("section", tok, None)
    return jax.shard_map(
        on_device, mesh=inner, in_specs=in_specs, out_specs=out_specs, check_vma=False
    )
```

```python
from functools import partial

import jax
import jax.numpy as jnp
import numpy as np
from jax import lax
from jax.sharding import Mesh
from jax.sharding import PartitionSpec as P

ALL = ("eg", "qa", "c", "dp")


def passed_along(array, axis, by):
    length = lax.axis_size(axis)
    return lax.ppermute(array, axis, [(i, (i + by) % length) for i in range(length)])


def route(stream, gain_row, routes, experts, capacity):
    tok_rows, model_width = stream.shape
    fan_out = routes.shape[1]
    widened = stream.astype(jnp.float32)
    inv_rms = lax.rsqrt(jnp.mean(widened * widened, axis=1, keepdims=True) + 1e-06)
    normed = (widened * inv_rms * gain_row[None, :]).astype(jnp.bfloat16)
    flat_ids = routes.reshape(-1)
    count_all = flat_ids.shape[0]
    chosen = (flat_ids[:, None] == jnp.arange(experts, dtype=jnp.int32)[None, :]).astype(
        jnp.float32
    )
    triangle = (jnp.arange(count_all)[:, None] >= jnp.arange(count_all)[None, :]).astype(
        jnp.float32
    )
    running = jnp.dot(triangle, chosen, preferred_element_type=jnp.float32)
    slot_of = jnp.sum(chosen * (running - 1.0), axis=1).astype(jnp.int32)
    target = flat_ids * capacity + slot_of
    placing = jnp.arange(experts * capacity, dtype=jnp.int32)[:, None] == target[None, :]
    placing = (
        placing.reshape(experts * capacity, tok_rows, fan_out).any(axis=2).astype(jnp.bfloat16)
    )
    outgoing = jnp.dot(placing, normed, preferred_element_type=jnp.float32).astype(jnp.bfloat16)
    return widened, outgoing.reshape(experts, capacity, model_width), target


def moe_layer(stream, gain_row, gate_w, up_w, down_mine, routes, mixing):
    experts = lax.axis_size("eg")
    blocks = lax.axis_size("qa") * lax.axis_size("c")
    halves = lax.axis_size("dp")
    tok_rows, model_width = stream.shape
    fan_out = routes.shape[1]
    capacity = min(tok_rows, max(2, 5 * tok_rows * fan_out // (4 * experts)))
    half = model_width // halves
    widened, outgoing, target = route(stream, gain_row, routes, experts, capacity)
    lanes = 128
    tiles = half // lanes
    send = outgoing.reshape(experts, capacity, halves, tiles, lanes).transpose(0, 2, 1, 3, 4)
    send = send.reshape(experts * halves, capacity * tiles, lanes)
    arrived = lax.all_to_all(send, ("eg", "dp"), split_axis=0, concat_axis=0, tiled=True)
    arrived = arrived.reshape(experts * halves, capacity, half).transpose(1, 0, 2)
    arrived = lax.all_gather(arrived, "qa", axis=1, tiled=True)
    arrived = lax.all_gather(arrived, "c", axis=1, tiled=True)
    sources = blocks * experts * halves
    rows = arrived.reshape(capacity * sources, half)
    gate_part = jnp.dot(rows, gate_w, preferred_element_type=jnp.float32)
    up_part = jnp.dot(rows, up_w, preferred_element_type=jnp.float32)
    mine = jnp.stack([gate_part, up_part])
    both = mine + passed_along(mine, "dp", 1)
    hidden = (jax.nn.silu(both[0]) * both[1]).astype(jnp.bfloat16)
    hidden_all = lax.all_gather(hidden, ("qa", "c"), axis=1, tiled=True)
    out = lax.dot_general(
        hidden_all, down_mine, (((1,), (1,)), ((), ())), preferred_element_type=jnp.float32
    ).astype(jnp.bfloat16)
    piece = out.shape[1]
    cores = lax.axis_size("c")
    out = out.reshape(capacity, cores, blocks // cores, experts, halves, piece)
    out = out.transpose(3, 2, 1, 4, 0, 5)
    back = lax.all_to_all(
        out.reshape(sources, capacity, piece), ALL, split_axis=0, concat_axis=0, tiled=True
    )
    back = back.reshape(experts, blocks, halves, capacity, piece).transpose(0, 3, 2, 1, 4)
    expert_out = back.reshape(experts * capacity, model_width)
    picked = jnp.take(expert_out, target, axis=0)
    picked = picked.reshape(tok_rows, fan_out, model_width)
    mixed_sum = jnp.sum(mixing[:, :, None] * picked.astype(jnp.float32), axis=1)
    return (widened + mixed_sum).astype(jnp.bfloat16)


def on_device(blocks, gains, w_gate, w_up, w_down, expert_ids, combine):
    stream = blocks[0]
    turns = expert_ids.shape[1]
    n_blocks = lax.axis_size("qa") * lax.axis_size("c")
    down_local = w_down[0]
    half, width = down_local.shape
    piece = half // n_blocks
    down_mine = lax.all_to_all(
        down_local.reshape(n_blocks, piece, width), ("qa", "c"), split_axis=0, concat_axis=0, tiled=True
    )
    down_mine = down_mine.transpose(1, 0, 2).reshape(piece, n_blocks * width)
    for layer_turn in range(turns):
        if layer_turn > 0:
            stream = passed_along(stream, "section", 1)
        stream = moe_layer(
            stream,
            gains[0],
            w_gate[0],
            w_up[0],
            down_mine,
            expert_ids[0, layer_turn],
            combine[0, layer_turn],
        )
    return stream[None]


def solution(mesh):
    n_section, n_expert, n_dp = (mesh.shape[a] for a in ("section", "expert", "dp"))
    n_q = n_expert // 4
    n_core = 2
    inner = Mesh(
        np.asarray(mesh.devices).reshape(n_section, n_expert // n_q, n_q // n_core, n_core, n_dp),
        ("section", "eg", "qa", "c", "dp"),
    )
    tok = ("eg", "qa", "c", "dp")
    in_specs = (
        P("section", tok, None),
        P("section", None),
        P("section", "dp", ("eg", "qa", "c")),
        P("section", "dp", ("eg", "qa", "c")),
        P("section", "dp", ("eg", "qa", "c")),
        P("section", None, tok, None),
        P("section", None, tok, None),
    )
    out_specs = P("section", tok, None)
    return jax.shard_map(
        on_device, mesh=inner, in_specs=in_specs, out_specs=out_specs, check_vma=False
    )
```

```python
from functools import partial

import jax
import jax.numpy as jnp
import numpy as np
from jax import lax
from jax.sharding import Mesh
from jax.sharding import PartitionSpec as P

ALL = ("eg", "q", "dp")


def passed_along(array, axis, by):
    length = lax.axis_size(axis)
    return lax.ppermute(array, axis, [(i, (i + by) % length) for i in range(length)])


def route(stream, gain_row, routes, experts, capacity):
    tok_rows, model_width = stream.shape
    fan_out = routes.shape[1]
    widened = stream.astype(jnp.float32)
    inv_rms = lax.rsqrt(jnp.mean(widened * widened, axis=1, keepdims=True) + 1e-06)
    normed = (widened * inv_rms * gain_row[None, :]).astype(jnp.bfloat16)
    flat_ids = routes.reshape(-1)
    count_all = flat_ids.shape[0]
    chosen = (flat_ids[:, None] == jnp.arange(experts, dtype=jnp.int32)[None, :]).astype(
        jnp.float32
    )
    triangle = (jnp.arange(count_all)[:, None] >= jnp.arange(count_all)[None, :]).astype(
        jnp.float32
    )
    running = jnp.dot(triangle, chosen, preferred_element_type=jnp.float32)
    slot_of = jnp.sum(chosen * (running - 1.0), axis=1).astype(jnp.int32)
    target = flat_ids * capacity + slot_of
    placing = jnp.arange(experts * capacity, dtype=jnp.int32)[:, None] == target[None, :]
    placing = (
        placing.reshape(experts * capacity, tok_rows, fan_out).any(axis=2).astype(jnp.bfloat16)
    )
    outgoing = jnp.dot(placing, normed, preferred_element_type=jnp.float32).astype(jnp.bfloat16)
    return widened, outgoing.reshape(experts, capacity, model_width), target


def expert_rows(outgoing, gate_w, up_w, down_mine):
    experts = lax.axis_size("eg")
    blocks = lax.axis_size("q")
    halves = lax.axis_size("dp")
    _, capacity, model_width = outgoing.shape
    half = model_width // halves
    lanes = 128
    tiles = half // lanes
    send = outgoing.reshape(experts, capacity, halves, tiles, lanes).transpose(0, 2, 1, 3, 4)
    send = send.reshape(experts * halves, capacity * tiles, lanes)
    arrived = lax.all_to_all(send, ("eg", "dp"), split_axis=0, concat_axis=0, tiled=True)
    arrived = arrived.reshape(experts * halves, capacity, half).transpose(1, 0, 2)
    arrived = lax.all_gather(arrived, "q", axis=1, tiled=True)
    sources = blocks * experts * halves
    rows = arrived.reshape(capacity * sources, half)
    gate_part = jnp.dot(rows, gate_w, preferred_element_type=jnp.float32)
    up_part = jnp.dot(rows, up_w, preferred_element_type=jnp.float32)
    mine = jnp.stack([gate_part, up_part])
    both = mine + passed_along(mine, "dp", 1)
    hidden = (jax.nn.silu(both[0]) * both[1]).astype(jnp.bfloat16)
    hidden_all = lax.all_gather(hidden, "q", axis=1, tiled=True)
    out = lax.dot_general(
        hidden_all, down_mine, (((1,), (1,)), ((), ())), preferred_element_type=jnp.float32
    ).astype(jnp.bfloat16)
    piece = out.shape[1]
    out = out.reshape(capacity, blocks, experts, halves, piece).transpose(2, 1, 3, 0, 4)
    back = lax.all_to_all(
        out.reshape(sources, capacity, piece), ALL, split_axis=0, concat_axis=0, tiled=True
    )
    back = back.reshape(experts, blocks, halves, capacity, piece).transpose(0, 3, 2, 1, 4)
    return back.reshape(experts, capacity, model_width)


def moe_layer(stream, gain_row, gate_w, up_w, down_mine, routes, mixing):
    experts = lax.axis_size("eg")
    tok_rows, model_width = stream.shape
    fan_out = routes.shape[1]
    capacity = min(tok_rows, max(2, 5 * tok_rows * fan_out // (4 * experts)))
    widened, outgoing, target = route(stream, gain_row, routes, experts, capacity)
    cut = (capacity + 1) // 2
    parts = [
        expert_rows(outgoing[:, :cut], gate_w, up_w, down_mine),
        expert_rows(outgoing[:, cut:], gate_w, up_w, down_mine),
    ]
    expert_out = jnp.concatenate(parts, axis=1).reshape(experts * capacity, model_width)
    picked = jnp.take(expert_out, target, axis=0)
    picked = picked.reshape(tok_rows, fan_out, model_width)
    mixed_sum = jnp.sum(mixing[:, :, None] * picked.astype(jnp.float32), axis=1)
    return (widened + mixed_sum).astype(jnp.bfloat16)


def on_device(blocks, gains, w_gate, w_up, w_down, expert_ids, combine):
    stream = blocks[0]
    turns = expert_ids.shape[1]
    n_blocks = lax.axis_size("q")
    down_local = w_down[0]
    half, width = down_local.shape
    piece = half // n_blocks
    down_mine = lax.all_to_all(
        down_local.reshape(n_blocks, piece, width), "q", split_axis=0, concat_axis=0, tiled=True
    )
    down_mine = down_mine.transpose(1, 0, 2).reshape(piece, n_blocks * width)
    for layer_turn in range(turns):
        if layer_turn > 0:
            stream = passed_along(stream, "section", 1)
        stream = moe_layer(
            stream,
            gains[0],
            w_gate[0],
            w_up[0],
            down_mine,
            expert_ids[0, layer_turn],
            combine[0, layer_turn],
        )
    return stream[None]


def solution(mesh):
    n_section, n_expert, n_dp = (mesh.shape[a] for a in ("section", "expert", "dp"))
    n_q = n_expert // 4
    inner = Mesh(
        np.asarray(mesh.devices).reshape(n_section, n_expert // n_q, n_q, n_dp),
        ("section", "eg", "q", "dp"),
    )
    tok = ("eg", "q", "dp")
    in_specs = (
        P("section", tok, None),
        P("section", None),
        P("section", "dp", ("eg", "q")),
        P("section", "dp", ("eg", "q")),
        P("section", "dp", ("eg", "q")),
        P("section", None, tok, None),
        P("section", None, tok, None),
    )
    out_specs = P("section", tok, None)
    return jax.shard_map(
        on_device, mesh=inner, in_specs=in_specs, out_specs=out_specs, check_vma=False
    )
```

```python
from functools import partial

import jax
import jax.numpy as jnp
import numpy as np
from jax import lax
from jax.sharding import Mesh
from jax.sharding import PartitionSpec as P

ALL = ("eg", "q", "dp")


def passed_along(array, axis, by):
    length = lax.axis_size(axis)
    return lax.ppermute(array, axis, [(i, (i + by) % length) for i in range(length)])


def route(stream, gain_row, routes, experts, capacity):
    tok_rows, model_width = stream.shape
    fan_out = routes.shape[1]
    widened = stream.astype(jnp.float32)
    inv_rms = lax.rsqrt(jnp.mean(widened * widened, axis=1, keepdims=True) + 1e-06)
    normed = (widened * inv_rms * gain_row[None, :]).astype(jnp.bfloat16)
    flat_ids = routes.reshape(-1)
    count_all = flat_ids.shape[0]
    chosen = (flat_ids[:, None] == jnp.arange(experts, dtype=jnp.int32)[None, :]).astype(
        jnp.float32
    )
    triangle = (jnp.arange(count_all)[:, None] >= jnp.arange(count_all)[None, :]).astype(
        jnp.float32
    )
    running = jnp.dot(triangle, chosen, preferred_element_type=jnp.float32)
    slot_of = jnp.sum(chosen * (running - 1.0), axis=1).astype(jnp.int32)
    target = flat_ids * capacity + slot_of
    placing = jnp.arange(experts * capacity, dtype=jnp.int32)[:, None] == target[None, :]
    placing = (
        placing.reshape(experts * capacity, tok_rows, fan_out).any(axis=2).astype(jnp.bfloat16)
    )
    outgoing = jnp.dot(placing, normed, preferred_element_type=jnp.float32).astype(jnp.bfloat16)
    return widened, outgoing.reshape(experts, capacity, model_width), target


def moe_layer(stream, gain_row, gate_w, up_w, down_mine, routes, mixing):
    experts = lax.axis_size("eg")
    blocks = lax.axis_size("q")
    halves = lax.axis_size("dp")
    tok_rows, model_width = stream.shape
    fan_out = routes.shape[1]
    capacity = min(tok_rows, max(2, 5 * tok_rows * fan_out // (4 * experts)))
    half = model_width // halves
    widened, outgoing, target = route(stream, gain_row, routes, experts, capacity)
    lanes = 128
    tiles = half // lanes
    send = outgoing.reshape(experts, capacity, halves, tiles, lanes).transpose(0, 2, 1, 3, 4)
    send = send.reshape(experts * halves, capacity * tiles, lanes)
    arrived = lax.all_to_all(send, ("eg", "dp"), split_axis=0, concat_axis=0, tiled=True)
    arrived = arrived.reshape(experts * halves, capacity, half).transpose(1, 0, 2)
    arrived = lax.all_gather(arrived, "q", axis=1, tiled=True)
    sources = blocks * experts * halves
    rows = arrived.reshape(capacity * sources, half)
    gate_part = jnp.dot(rows, gate_w, preferred_element_type=jnp.float32)
    up_part = jnp.dot(rows, up_w, preferred_element_type=jnp.float32)
    mine = jnp.stack([gate_part, up_part])
    share = mine.shape[1] // halves
    side = lax.axis_index("dp")
    keep = lax.dynamic_slice_in_dim(mine, side * share, share, axis=1)
    give = lax.dynamic_slice_in_dim(mine, (1 - side) * share, share, axis=1)
    both = keep + passed_along(give, "dp", 1)
    hidden = (jax.nn.silu(both[0]) * both[1]).astype(jnp.bfloat16)
    units = hidden.shape[1]
    hidden_all = lax.all_gather(hidden, ("q", "dp"), axis=0, tiled=False)
    hidden_all = hidden_all.reshape(blocks, halves, share, units).transpose(1, 2, 0, 3)
    hidden_all = hidden_all.reshape(halves * share, blocks * units)
    out = lax.dot_general(
        hidden_all, down_mine, (((1,), (1,)), ((), ())), preferred_element_type=jnp.float32
    ).astype(jnp.bfloat16)
    piece = out.shape[1]
    out = out.reshape(capacity, blocks, experts, halves, piece).transpose(2, 1, 3, 0, 4)
    back = lax.all_to_all(
        out.reshape(sources, capacity, piece), ALL, split_axis=0, concat_axis=0, tiled=True
    )
    back = back.reshape(experts, blocks, halves, capacity, piece).transpose(0, 3, 2, 1, 4)
    expert_out = back.reshape(experts * capacity, model_width)
    picked = jnp.take(expert_out, target, axis=0)
    picked = picked.reshape(tok_rows, fan_out, model_width)
    mixed_sum = jnp.sum(mixing[:, :, None] * picked.astype(jnp.float32), axis=1)
    return (widened + mixed_sum).astype(jnp.bfloat16)


def on_device(blocks, gains, w_gate, w_up, w_down, expert_ids, combine):
    stream = blocks[0]
    turns = expert_ids.shape[1]
    n_blocks = lax.axis_size("q")
    down_local = w_down[0]
    half, width = down_local.shape
    piece = half // n_blocks
    down_mine = lax.all_to_all(
        down_local.reshape(n_blocks, piece, width), "q", split_axis=0, concat_axis=0, tiled=True
    )
    down_mine = down_mine.transpose(1, 0, 2).reshape(piece, n_blocks * width)
    for layer_turn in range(turns):
        if layer_turn > 0:
            stream = passed_along(stream, "section", 1)
        stream = moe_layer(
            stream,
            gains[0],
            w_gate[0],
            w_up[0],
            down_mine,
            expert_ids[0, layer_turn],
            combine[0, layer_turn],
        )
    return stream[None]


def solution(mesh):
    n_section, n_expert, n_dp = (mesh.shape[a] for a in ("section", "expert", "dp"))
    n_q = n_expert // 4
    inner = Mesh(
        np.asarray(mesh.devices).reshape(n_section, n_expert // n_q, n_q, n_dp),
        ("section", "eg", "q", "dp"),
    )
    tok = ("eg", "q", "dp")
    in_specs = (
        P("section", tok, None),
        P("section", None),
        P("section", "dp", ("eg", "q")),
        P("section", "dp", ("eg", "q")),
        P("section", "dp", ("eg", "q")),
        P("section", None, tok, None),
        P("section", None, tok, None),
    )
    out_specs = P("section", tok, None)
    return jax.shard_map(
        on_device, mesh=inner, in_specs=in_specs, out_specs=out_specs, check_vma=False
    )
```

```python
from functools import partial

import jax
import jax.numpy as jnp
import numpy as np
from jax import lax
from jax.sharding import Mesh
from jax.sharding import PartitionSpec as P

ALL = ("eg", "q", "dp")


def passed_along(array, axis, by):
    length = lax.axis_size(axis)
    return lax.ppermute(array, axis, [(i, (i + by) % length) for i in range(length)])


def route(stream, gain_row, routes, experts, capacity):
    tok_rows, model_width = stream.shape
    fan_out = routes.shape[1]
    widened = stream.astype(jnp.float32)
    inv_rms = lax.rsqrt(jnp.mean(widened * widened, axis=1, keepdims=True) + 1e-06)
    normed = (widened * inv_rms * gain_row[None, :]).astype(jnp.bfloat16)
    flat_ids = routes.reshape(-1)
    count_all = flat_ids.shape[0]
    chosen = (flat_ids[:, None] == jnp.arange(experts, dtype=jnp.int32)[None, :]).astype(
        jnp.float32
    )
    triangle = (jnp.arange(count_all)[:, None] >= jnp.arange(count_all)[None, :]).astype(
        jnp.float32
    )
    running = jnp.dot(triangle, chosen, preferred_element_type=jnp.float32)
    slot_of = jnp.sum(chosen * (running - 1.0), axis=1).astype(jnp.int32)
    target = flat_ids * capacity + slot_of
    placing = jnp.arange(experts * capacity, dtype=jnp.int32)[:, None] == target[None, :]
    placing = (
        placing.reshape(experts * capacity, tok_rows, fan_out).any(axis=2).astype(jnp.bfloat16)
    )
    outgoing = jnp.dot(placing, normed, preferred_element_type=jnp.float32).astype(jnp.bfloat16)
    return widened, outgoing.reshape(experts, capacity, model_width), target


def moe_layer(stream, gain_row, gate_w, up_w, down_mine, routes, mixing):
    experts = lax.axis_size("eg")
    blocks = lax.axis_size("q")
    halves = lax.axis_size("dp")
    tok_rows, model_width = stream.shape
    fan_out = routes.shape[1]
    capacity = min(tok_rows, max(2, 5 * tok_rows * fan_out // (4 * experts)))
    half = model_width // halves
    widened, outgoing, target = route(stream, gain_row, routes, experts, capacity)
    lanes = 128
    tiles = half // lanes
    send = outgoing.reshape(experts, capacity, halves, tiles, lanes).transpose(0, 2, 1, 3, 4)
    send = send.reshape(experts * halves, capacity * tiles, lanes)
    arrived = lax.all_to_all(send, ("eg", "dp"), split_axis=0, concat_axis=0, tiled=True)
    arrived = arrived.reshape(experts * halves, capacity, half).transpose(1, 0, 2)
    arrived = lax.all_gather(arrived, "q", axis=1, tiled=True)
    sources = blocks * experts * halves
    rows = arrived.reshape(capacity * sources, half)
    gate_part = jnp.dot(rows, gate_w, preferred_element_type=jnp.float32)
    up_part = jnp.dot(rows, up_w, preferred_element_type=jnp.float32)
    mine = jnp.stack([gate_part, up_part])
    both = mine + passed_along(mine, "dp", 1)
    hidden = (jax.nn.silu(both[0]) * both[1]).astype(jnp.bfloat16)
    hidden_all = lax.all_gather(hidden, "q", axis=1, tiled=True)
    out = lax.dot_general(
        hidden_all, down_mine, (((1,), (1,)), ((), ())), preferred_element_type=jnp.float32
    ).astype(jnp.bfloat16)
    piece = out.shape[1]
    out = out.reshape(capacity, blocks, experts, halves, piece).transpose(2, 1, 3, 0, 4)
    back = lax.all_to_all(
        out.reshape(sources, 2, capacity * piece // 2), ALL, split_axis=0, concat_axis=0, tiled=True
    )
    back = back.reshape(experts, blocks, halves, capacity, piece).transpose(0, 3, 2, 1, 4)
    expert_out = back.reshape(experts * capacity, model_width)
    picked = jnp.take(expert_out, target, axis=0)
    picked = picked.reshape(tok_rows, fan_out, model_width)
    mixed_sum = jnp.sum(mixing[:, :, None] * picked.astype(jnp.float32), axis=1)
    return (widened + mixed_sum).astype(jnp.bfloat16)


def on_device(blocks, gains, w_gate, w_up, w_down, expert_ids, combine):
    stream = blocks[0]
    turns = expert_ids.shape[1]
    n_blocks = lax.axis_size("q")
    down_local = w_down[0]
    half, width = down_local.shape
    piece = half // n_blocks
    down_mine = lax.all_to_all(
        down_local.reshape(n_blocks, piece, width), "q", split_axis=0, concat_axis=0, tiled=True
    )
    down_mine = down_mine.transpose(1, 0, 2).reshape(piece, n_blocks * width)
    for layer_turn in range(turns):
        if layer_turn > 0:
            stream = passed_along(stream, "section", 1)
        stream = moe_layer(
            stream,
            gains[0],
            w_gate[0],
            w_up[0],
            down_mine,
            expert_ids[0, layer_turn],
            combine[0, layer_turn],
        )
    return stream[None]


def solution(mesh):
    n_section, n_expert, n_dp = (mesh.shape[a] for a in ("section", "expert", "dp"))
    n_q = n_expert // 4
    inner = Mesh(
        np.asarray(mesh.devices).reshape(n_section, n_expert // n_q, n_q, n_dp),
        ("section", "eg", "q", "dp"),
    )
    tok = ("eg", "q", "dp")
    in_specs = (
        P("section", tok, None),
        P("section", None),
        P("section", "dp", ("eg", "q")),
        P("section", "dp", ("eg", "q")),
        P("section", "dp", ("eg", "q")),
        P("section", None, tok, None),
        P("section", None, tok, None),
    )
    out_specs = P("section", tok, None)
    return jax.shard_map(
        on_device, mesh=inner, in_specs=in_specs, out_specs=out_specs, check_vma=False
    )
```

```python
from functools import partial

import jax
import jax.numpy as jnp
import numpy as np
from jax import lax
from jax.sharding import Mesh
from jax.sharding import PartitionSpec as P

ALL = ("eg", "q", "dp")


def passed_along(array, axis, by):
    length = lax.axis_size(axis)
    return lax.ppermute(array, axis, [(i, (i + by) % length) for i in range(length)])


def route(stream, gain_row, routes, experts, capacity):
    tok_rows, model_width = stream.shape
    fan_out = routes.shape[1]
    widened = stream.astype(jnp.float32)
    inv_rms = lax.rsqrt(jnp.mean(widened * widened, axis=1, keepdims=True) + 1e-06)
    normed = (widened * inv_rms * gain_row[None, :]).astype(jnp.bfloat16)
    flat_ids = routes.reshape(-1)
    count_all = flat_ids.shape[0]
    chosen = (flat_ids[:, None] == jnp.arange(experts, dtype=jnp.int32)[None, :]).astype(
        jnp.float32
    )
    triangle = (jnp.arange(count_all)[:, None] >= jnp.arange(count_all)[None, :]).astype(
        jnp.float32
    )
    running = jnp.dot(triangle, chosen, preferred_element_type=jnp.float32)
    slot_of = jnp.sum(chosen * (running - 1.0), axis=1).astype(jnp.int32)
    target = flat_ids * capacity + slot_of
    placing = jnp.arange(experts * capacity, dtype=jnp.int32)[:, None] == target[None, :]
    placing = (
        placing.reshape(experts * capacity, tok_rows, fan_out).any(axis=2).astype(jnp.bfloat16)
    )
    outgoing = jnp.dot(placing, normed, preferred_element_type=jnp.float32).astype(jnp.bfloat16)
    return widened, outgoing.reshape(experts, capacity, model_width), target


def moe_layer(stream, gain_row, gate_w, up_w, down_mine, routes, mixing):
    experts = lax.axis_size("eg")
    blocks = lax.axis_size("q")
    halves = lax.axis_size("dp")
    tok_rows, model_width = stream.shape
    fan_out = routes.shape[1]
    capacity = min(tok_rows, max(2, 5 * tok_rows * fan_out // (4 * experts)))
    half = model_width // halves
    widened, outgoing, target = route(stream, gain_row, routes, experts, capacity)
    lanes = 128
    tiles = half // lanes
    send = outgoing.reshape(experts, capacity, halves, tiles, lanes).transpose(0, 2, 1, 3, 4)
    send = send.reshape(experts * halves, capacity * tiles, lanes)
    arrived = lax.all_to_all(send, ("eg", "dp"), split_axis=0, concat_axis=0, tiled=True)
    arrived = arrived.reshape(experts * halves, capacity, half).transpose(1, 0, 2)
    arrived = lax.all_gather(arrived, "q", axis=1, tiled=True)
    sources = blocks * experts * halves
    rows = arrived.reshape(capacity * sources, half)
    gate_part = jnp.dot(rows, gate_w, preferred_element_type=jnp.float32)
    up_part = jnp.dot(rows, up_w, preferred_element_type=jnp.float32)
    mine = jnp.stack([gate_part, up_part])
    both = mine + passed_along(mine, "dp", 1)
    hidden = (jax.nn.silu(both[0]) * both[1]).astype(jnp.bfloat16)
    hidden_all = lax.all_gather(hidden, "q", axis=1, tiled=True)
    out = lax.dot_general(
        hidden_all, down_mine, (((1,), (1,)), ((), ())), preferred_element_type=jnp.float32
    ).astype(jnp.bfloat16)
    piece = out.shape[1]
    out = out.reshape(capacity, blocks, experts, halves, piece).transpose(2, 1, 3, 0, 4)
    back = lax.all_to_all(
        out.reshape(sources, 2, capacity * piece // 2), ALL, split_axis=0, concat_axis=0, tiled=True
    )
    back = back.reshape(experts, blocks, halves, capacity, piece).transpose(0, 3, 2, 1, 4)
    expert_out = back.reshape(experts * capacity, model_width)
    picked = jnp.take(expert_out, target, axis=0)
    picked = picked.reshape(tok_rows, fan_out, model_width)
    mixed_sum = jnp.sum(mixing[:, :, None] * picked.astype(jnp.float32), axis=1)
    return (widened + mixed_sum).astype(jnp.bfloat16)


def moe_layer_rows(stream, gain_row, gate_full, up_full, down_rows, routes, mixing):
    experts = lax.axis_size("eg")
    blocks = lax.axis_size("q")
    halves = lax.axis_size("dp")
    tok_rows, model_width = stream.shape
    fan_out = routes.shape[1]
    capacity = min(tok_rows, max(2, 5 * tok_rows * fan_out // (4 * experts)))
    widened, outgoing, target = route(stream, gain_row, routes, experts, capacity)
    lanes = 128
    tiles = model_width // lanes
    send = outgoing.reshape(experts, capacity * tiles, lanes)
    arrived = lax.all_to_all(send, "eg", split_axis=0, concat_axis=0, tiled=True)
    arrived = arrived.reshape(experts, capacity, model_width).transpose(1, 0, 2)
    arrived = lax.all_gather(arrived, "q", axis=1, tiled=True)
    sources = blocks * experts
    rows = arrived.reshape(capacity * sources, model_width)
    gate_act = jnp.dot(rows, gate_full, preferred_element_type=jnp.float32)
    upward = jnp.dot(rows, up_full, preferred_element_type=jnp.float32)
    hidden = (jax.nn.silu(gate_act) * upward).astype(jnp.bfloat16)
    hidden_all = lax.all_gather(hidden, "q", axis=1, tiled=True)
    out = lax.dot_general(
        hidden_all, down_rows, (((1,), (1,)), ((), ())), preferred_element_type=jnp.float32
    ).astype(jnp.bfloat16)
    piece = out.shape[1]
    out = out.reshape(capacity, blocks, experts, piece).transpose(2, 1, 0, 3)
    back = lax.all_to_all(
        out.reshape(sources, 2, capacity * piece // 2), ("eg", "q"), split_axis=0, concat_axis=0,
        tiled=True,
    )
    sub = piece // halves
    back = back.reshape(experts, blocks, capacity, halves, sub).transpose(0, 2, 3, 1, 4)
    expert_out = back.reshape(experts * capacity, model_width)
    picked = jnp.take(expert_out, target, axis=0)
    picked = picked.reshape(tok_rows, fan_out, model_width)
    mixed_sum = jnp.sum(mixing[:, :, None] * picked.astype(jnp.float32), axis=1)
    return (widened + mixed_sum).astype(jnp.bfloat16)


def in_order(first, mine, other):
    return jnp.where(first, jnp.concatenate([mine, other]), jnp.concatenate([other, mine]))


def on_device(blocks, gains, w_gate, w_up, w_down, expert_ids, combine):
    stream = blocks[0]
    turns = expert_ids.shape[1]
    n_blocks = lax.axis_size("q")
    down_local = w_down[0]
    half, width = down_local.shape
    piece = half // n_blocks
    down_mine = lax.all_to_all(
        down_local.reshape(n_blocks, piece, width), "q", split_axis=0, concat_axis=0, tiled=True
    )
    down_mine = down_mine.transpose(1, 0, 2).reshape(piece, n_blocks * width)
    first = lax.axis_index("dp") == 0
    other = passed_along(jnp.stack([w_gate[0], w_up[0]]), "dp", 1)
    other_down = passed_along(down_mine, "dp", 1)
    for layer_turn in range(turns):
        if layer_turn > 0:
            stream, other, other_down = lax.optimization_barrier((stream, other, other_down))
            stream = passed_along(stream, "section", 1)
            stream = moe_layer_rows(
                stream,
                gains[0],
                in_order(first, w_gate[0], other[0]),
                in_order(first, w_up[0], other[1]),
                in_order(first, down_mine, other_down),
                expert_ids[0, layer_turn],
                combine[0, layer_turn],
            )
            continue
        stream = moe_layer(
            stream,
            gains[0],
            w_gate[0],
            w_up[0],
            down_mine,
            expert_ids[0, layer_turn],
            combine[0, layer_turn],
        )
    return stream[None]


def solution(mesh):
    n_section, n_expert, n_dp = (mesh.shape[a] for a in ("section", "expert", "dp"))
    n_q = n_expert // 4
    inner = Mesh(
        np.asarray(mesh.devices).reshape(n_section, n_expert // n_q, n_q, n_dp),
        ("section", "eg", "q", "dp"),
    )
    tok = ("eg", "q", "dp")
    in_specs = (
        P("section", tok, None),
        P("section", None),
        P("section", "dp", ("eg", "q")),
        P("section", "dp", ("eg", "q")),
        P("section", "dp", ("eg", "q")),
        P("section", None, tok, None),
        P("section", None, tok, None),
    )
    out_specs = P("section", tok, None)
    return jax.shard_map(
        on_device, mesh=inner, in_specs=in_specs, out_specs=out_specs, check_vma=False
    )
```

```python
from functools import partial

import jax
import jax.numpy as jnp
import numpy as np
from jax import lax
from jax.sharding import Mesh
from jax.sharding import PartitionSpec as P

ALL = ("eg", "q", "dp")


def passed_along(array, axis, by):
    length = lax.axis_size(axis)
    return lax.ppermute(array, axis, [(i, (i + by) % length) for i in range(length)])


def route(stream, gain_row, routes, experts, capacity):
    tok_rows, model_width = stream.shape
    fan_out = routes.shape[1]
    widened = stream.astype(jnp.float32)
    inv_rms = lax.rsqrt(jnp.mean(widened * widened, axis=1, keepdims=True) + 1e-06)
    normed = (widened * inv_rms * gain_row[None, :]).astype(jnp.bfloat16)
    flat_ids = routes.reshape(-1)
    count_all = flat_ids.shape[0]
    chosen = (flat_ids[:, None] == jnp.arange(experts, dtype=jnp.int32)[None, :]).astype(
        jnp.float32
    )
    triangle = (jnp.arange(count_all)[:, None] >= jnp.arange(count_all)[None, :]).astype(
        jnp.float32
    )
    running = jnp.dot(triangle, chosen, preferred_element_type=jnp.float32)
    slot_of = jnp.sum(chosen * (running - 1.0), axis=1).astype(jnp.int32)
    target = flat_ids * capacity + slot_of
    placing = jnp.arange(experts * capacity, dtype=jnp.int32)[:, None] == target[None, :]
    placing = (
        placing.reshape(experts * capacity, tok_rows, fan_out).any(axis=2).astype(jnp.bfloat16)
    )
    outgoing = jnp.dot(placing, normed, preferred_element_type=jnp.float32).astype(jnp.bfloat16)
    return widened, outgoing.reshape(experts, capacity, model_width), target


def moe_layer(stream, gain_row, gate_w, up_w, down_mine, routes, mixing):
    experts = lax.axis_size("eg")
    blocks = lax.axis_size("q")
    halves = lax.axis_size("dp")
    tok_rows, model_width = stream.shape
    fan_out = routes.shape[1]
    capacity = min(tok_rows, max(2, 5 * tok_rows * fan_out // (4 * experts)))
    half = model_width // halves
    widened, outgoing, target = route(stream, gain_row, routes, experts, capacity)
    lanes = 128
    tiles = half // lanes
    send = outgoing.reshape(experts, capacity, halves, tiles, lanes).transpose(0, 2, 1, 3, 4)
    send = send.reshape(experts * halves, capacity * tiles, lanes)
    arrived = lax.all_to_all(send, ("eg", "dp"), split_axis=0, concat_axis=0, tiled=True)
    arrived = arrived.reshape(experts * halves, capacity, half).transpose(1, 0, 2)
    arrived = lax.all_gather(arrived, "q", axis=1, tiled=True)
    sources = blocks * experts * halves
    rows = arrived.reshape(capacity * sources, half)
    gate_part = jnp.dot(rows, gate_w, preferred_element_type=jnp.float32)
    up_part = jnp.dot(rows, up_w, preferred_element_type=jnp.float32)
    mine = jnp.stack([gate_part, up_part])
    both = mine + passed_along(mine.astype(jnp.bfloat16), "dp", 1).astype(jnp.float32)
    hidden = (jax.nn.silu(both[0]) * both[1]).astype(jnp.bfloat16)
    hidden_all = lax.all_gather(hidden, "q", axis=1, tiled=True)
    out = lax.dot_general(
        hidden_all, down_mine, (((1,), (1,)), ((), ())), preferred_element_type=jnp.float32
    ).astype(jnp.bfloat16)
    piece = out.shape[1]
    out = out.reshape(capacity, blocks, experts, halves, piece).transpose(2, 1, 3, 0, 4)
    back = lax.all_to_all(
        out.reshape(sources, 2, capacity * piece // 2), ALL, split_axis=0, concat_axis=0, tiled=True
    )
    back = back.reshape(experts, blocks, halves, capacity, piece).transpose(0, 3, 2, 1, 4)
    expert_out = back.reshape(experts * capacity, model_width)
    picked = jnp.take(expert_out, target, axis=0)
    picked = picked.reshape(tok_rows, fan_out, model_width)
    mixed_sum = jnp.sum(mixing[:, :, None] * picked.astype(jnp.float32), axis=1)
    return (widened + mixed_sum).astype(jnp.bfloat16)


def on_device(blocks, gains, w_gate, w_up, w_down, expert_ids, combine):
    stream = blocks[0]
    turns = expert_ids.shape[1]
    n_blocks = lax.axis_size("q")
    down_local = w_down[0]
    half, width = down_local.shape
    piece = half // n_blocks
    down_mine = lax.all_to_all(
        down_local.reshape(n_blocks, piece, width), "q", split_axis=0, concat_axis=0, tiled=True
    )
    down_mine = down_mine.transpose(1, 0, 2).reshape(piece, n_blocks * width)
    for layer_turn in range(turns):
        if layer_turn > 0:
            stream = passed_along(stream, "section", 1)
        stream = moe_layer(
            stream,
            gains[0],
            w_gate[0],
            w_up[0],
            down_mine,
            expert_ids[0, layer_turn],
            combine[0, layer_turn],
        )
    return stream[None]


def solution(mesh):
    n_section, n_expert, n_dp = (mesh.shape[a] for a in ("section", "expert", "dp"))
    n_q = n_expert // 4
    inner = Mesh(
        np.asarray(mesh.devices).reshape(n_section, n_expert // n_q, n_q, n_dp),
        ("section", "eg", "q", "dp"),
    )
    tok = ("eg", "q", "dp")
    in_specs = (
        P("section", tok, None),
        P("section", None),
        P("section", "dp", ("eg", "q")),
        P("section", "dp", ("eg", "q")),
        P("section", "dp", ("eg", "q")),
        P("section", None, tok, None),
        P("section", None, tok, None),
    )
    out_specs = P("section", tok, None)
    return jax.shard_map(
        on_device, mesh=inner, in_specs=in_specs, out_specs=out_specs, check_vma=False
    )
```

```python
from functools import partial

import jax
import jax.numpy as jnp
import numpy as np
from jax import lax
from jax.sharding import Mesh
from jax.sharding import PartitionSpec as P

ALL = ("eg", "q", "dp")


def passed_along(array, axis, by):
    length = lax.axis_size(axis)
    return lax.ppermute(array, axis, [(i, (i + by) % length) for i in range(length)])


def route(stream, gain_row, routes, experts, capacity):
    tok_rows, model_width = stream.shape
    fan_out = routes.shape[1]
    widened = stream.astype(jnp.float32)
    inv_rms = lax.rsqrt(jnp.mean(widened * widened, axis=1, keepdims=True) + 1e-06)
    normed = (widened * inv_rms * gain_row[None, :]).astype(jnp.bfloat16)
    flat_ids = routes.reshape(-1)
    count_all = flat_ids.shape[0]
    chosen = (flat_ids[:, None] == jnp.arange(experts, dtype=jnp.int32)[None, :]).astype(
        jnp.float32
    )
    triangle = (jnp.arange(count_all)[:, None] >= jnp.arange(count_all)[None, :]).astype(
        jnp.float32
    )
    running = jnp.dot(triangle, chosen, preferred_element_type=jnp.float32)
    slot_of = jnp.sum(chosen * (running - 1.0), axis=1).astype(jnp.int32)
    target = flat_ids * capacity + slot_of
    placing = jnp.arange(experts * capacity, dtype=jnp.int32)[:, None] == target[None, :]
    placing = (
        placing.reshape(experts * capacity, tok_rows, fan_out).any(axis=2).astype(jnp.bfloat16)
    )
    outgoing = jnp.dot(placing, normed, preferred_element_type=jnp.float32).astype(jnp.bfloat16)
    return widened, outgoing.reshape(experts, capacity, model_width), target


def moe_layer(stream, gain_row, gate_w, up_w, down_mine, routes, mixing):
    experts = lax.axis_size("eg")
    blocks = lax.axis_size("q")
    halves = lax.axis_size("dp")
    tok_rows, model_width = stream.shape
    fan_out = routes.shape[1]
    capacity = min(tok_rows, max(2, 5 * tok_rows * fan_out // (4 * experts)))
    half = model_width // halves
    widened, outgoing, target = route(stream, gain_row, routes, experts, capacity)
    lanes = 128
    tiles = half // lanes
    send = outgoing.reshape(experts, capacity, halves, tiles, lanes).transpose(0, 2, 1, 3, 4)
    send = send.reshape(experts * halves, capacity * tiles, lanes)
    arrived = lax.all_to_all(send, ("eg", "dp"), split_axis=0, concat_axis=0, tiled=True)
    arrived = arrived.reshape(experts * halves, capacity, half).transpose(1, 0, 2)
    arrived = lax.all_gather(arrived, "q", axis=1, tiled=True)
    sources = blocks * experts * halves
    rows = arrived.reshape(capacity * sources, half)
    gate_part = jnp.dot(rows, gate_w, preferred_element_type=jnp.float32)
    up_part = jnp.dot(rows, up_w, preferred_element_type=jnp.float32)
    mine = jnp.stack([gate_part, up_part])
    both = mine + passed_along(mine.astype(jnp.bfloat16), "dp", 1).astype(jnp.float32)
    hidden = (jax.nn.silu(both[0]) * both[1]).astype(jnp.bfloat16)
    units = hidden.shape[1]
    hidden_all = lax.all_gather(hidden.reshape(capacity, sources, units), "q", axis=1, tiled=True)
    hidden_all = hidden_all.reshape(capacity, blocks, sources, units).transpose(0, 2, 1, 3)
    hidden_all = hidden_all.reshape(capacity * sources, blocks * units)
    out = lax.dot_general(
        hidden_all, down_mine, (((1,), (1,)), ((), ())), preferred_element_type=jnp.float32
    ).astype(jnp.bfloat16)
    piece = out.shape[1]
    out = out.reshape(capacity, blocks, experts, halves, piece).transpose(2, 1, 3, 0, 4)
    back = lax.all_to_all(
        out.reshape(sources, 2, capacity * piece // 2), ALL, split_axis=0, concat_axis=0, tiled=True
    )
    back = back.reshape(experts, blocks, halves, capacity, piece).transpose(0, 3, 2, 1, 4)
    expert_out = back.reshape(experts * capacity, model_width)
    picked = jnp.take(expert_out, target, axis=0)
    picked = picked.reshape(tok_rows, fan_out, model_width)
    mixed_sum = jnp.sum(mixing[:, :, None] * picked.astype(jnp.float32), axis=1)
    return (widened + mixed_sum).astype(jnp.bfloat16)


def on_device(blocks, gains, w_gate, w_up, w_down, expert_ids, combine):
    stream = blocks[0]
    turns = expert_ids.shape[1]
    n_blocks = lax.axis_size("q")
    down_local = w_down[0]
    half, width = down_local.shape
    piece = half // n_blocks
    down_mine = lax.all_to_all(
        down_local.reshape(n_blocks, piece, width), "q", split_axis=0, concat_axis=0, tiled=True
    )
    down_mine = down_mine.transpose(1, 0, 2).reshape(piece, n_blocks * width)
    for layer_turn in range(turns):
        if layer_turn > 0:
            stream = passed_along(stream, "section", 1)
        stream = moe_layer(
            stream,
            gains[0],
            w_gate[0],
            w_up[0],
            down_mine,
            expert_ids[0, layer_turn],
            combine[0, layer_turn],
        )
    return stream[None]


def solution(mesh):
    n_section, n_expert, n_dp = (mesh.shape[a] for a in ("section", "expert", "dp"))
    n_q = n_expert // 4
    inner = Mesh(
        np.asarray(mesh.devices).reshape(n_section, n_expert // n_q, n_q, n_dp),
        ("section", "eg", "q", "dp"),
    )
    tok = ("eg", "q", "dp")
    in_specs = (
        P("section", tok, None),
        P("section", None),
        P("section", "dp", ("eg", "q")),
        P("section", "dp", ("eg", "q")),
        P("section", "dp", ("eg", "q")),
        P("section", None, tok, None),
        P("section", None, tok, None),
    )
    out_specs = P("section", tok, None)
    return jax.shard_map(
        on_device, mesh=inner, in_specs=in_specs, out_specs=out_specs, check_vma=False
    )
```

```python
from functools import partial

import jax
import jax.numpy as jnp
import numpy as np
from jax import lax
from jax.sharding import Mesh
from jax.sharding import PartitionSpec as P

ALL = ("eg", "q", "dp")


def passed_along(array, axis, by):
    length = lax.axis_size(axis)
    return lax.ppermute(array, axis, [(i, (i + by) % length) for i in range(length)])


def route(stream, gain_row, routes, experts, capacity):
    tok_rows, model_width = stream.shape
    fan_out = routes.shape[1]
    widened = stream.astype(jnp.float32)
    inv_rms = lax.rsqrt(jnp.mean(widened * widened, axis=1, keepdims=True) + 1e-06)
    normed = (widened * inv_rms * gain_row[None, :]).astype(jnp.bfloat16)
    flat_ids = routes.reshape(-1)
    count_all = flat_ids.shape[0]
    chosen = (flat_ids[:, None] == jnp.arange(experts, dtype=jnp.int32)[None, :]).astype(
        jnp.float32
    )
    triangle = (jnp.arange(count_all)[:, None] >= jnp.arange(count_all)[None, :]).astype(
        jnp.float32
    )
    running = jnp.dot(triangle, chosen, preferred_element_type=jnp.float32)
    slot_of = jnp.sum(chosen * (running - 1.0), axis=1).astype(jnp.int32)
    target = flat_ids * capacity + slot_of
    placing = jnp.arange(experts * capacity, dtype=jnp.int32)[:, None] == target[None, :]
    placing = (
        placing.reshape(experts * capacity, tok_rows, fan_out).any(axis=2).astype(jnp.bfloat16)
    )
    outgoing = jnp.dot(placing, normed, preferred_element_type=jnp.float32).astype(jnp.bfloat16)
    return widened, outgoing.reshape(experts, capacity, model_width), target


def moe_layer(stream, gain_row, gate_w, up_w, down_mine, routes, mixing):
    experts = lax.axis_size("eg")
    blocks = lax.axis_size("q")
    halves = lax.axis_size("dp")
    tok_rows, model_width = stream.shape
    fan_out = routes.shape[1]
    capacity = min(tok_rows, max(2, 5 * tok_rows * fan_out // (4 * experts)))
    half = model_width // halves
    widened, outgoing, target = route(stream, gain_row, routes, experts, capacity)
    lanes = 128
    tiles = half // lanes
    send = outgoing.reshape(experts, capacity, halves, tiles, lanes).transpose(0, 2, 1, 3, 4)
    send = send.reshape(experts * halves, 2, capacity * half // 2)
    arrived = lax.all_to_all(send, ("eg", "dp"), split_axis=0, concat_axis=0, tiled=True)
    arrived = arrived.reshape(experts * halves, capacity, half).transpose(1, 0, 2)
    arrived = lax.all_gather(arrived, "q", axis=1, tiled=True)
    sources = blocks * experts * halves
    rows = arrived.reshape(capacity * sources, half)
    units = gate_w.shape[1]
    both_w = jnp.concatenate([gate_w, up_w], axis=1)
    gate_up = jnp.dot(rows, both_w, preferred_element_type=jnp.float32)
    mine = gate_up.reshape(rows.shape[0], 2, units).transpose(1, 0, 2)
    both = mine + passed_along(mine.astype(jnp.bfloat16), "dp", 1).astype(jnp.float32)
    hidden = (jax.nn.silu(both[0]) * both[1]).astype(jnp.bfloat16)
    hidden_all = lax.all_gather(hidden, "q", axis=1, tiled=True)
    out = lax.dot_general(
        hidden_all, down_mine, (((1,), (1,)), ((), ())), preferred_element_type=jnp.float32
    ).astype(jnp.bfloat16)
    piece = out.shape[1]
    out = out.reshape(capacity, blocks, experts, halves, piece).transpose(2, 1, 3, 0, 4)
    back = lax.all_to_all(
        out.reshape(sources, 2, capacity * piece // 2), ALL, split_axis=0, concat_axis=0, tiled=True
    )
    back = back.reshape(experts, blocks, halves, capacity, piece).transpose(0, 3, 2, 1, 4)
    expert_out = back.reshape(experts * capacity, model_width)
    picked = jnp.take(expert_out, target, axis=0)
    picked = picked.reshape(tok_rows, fan_out, model_width)
    mixed_sum = jnp.sum(mixing[:, :, None] * picked.astype(jnp.float32), axis=1)
    return (widened + mixed_sum).astype(jnp.bfloat16)


def on_device(blocks, gains, w_gate, w_up, w_down, expert_ids, combine):
    stream = blocks[0]
    turns = expert_ids.shape[1]
    n_blocks = lax.axis_size("q")
    down_local = w_down[0]
    half, width = down_local.shape
    piece = half // n_blocks
    down_mine = lax.all_to_all(
        down_local.reshape(n_blocks, piece, width), "q", split_axis=0, concat_axis=0, tiled=True
    )
    down_mine = down_mine.transpose(1, 0, 2).reshape(piece, n_blocks * width)
    for layer_turn in range(turns):
        if layer_turn > 0:
            stream = passed_along(stream, "section", 1)
        stream = moe_layer(
            stream,
            gains[0],
            w_gate[0],
            w_up[0],
            down_mine,
            expert_ids[0, layer_turn],
            combine[0, layer_turn],
        )
    return stream[None]


def solution(mesh):
    n_section, n_expert, n_dp = (mesh.shape[a] for a in ("section", "expert", "dp"))
    n_q = n_expert // 4
    inner = Mesh(
        np.asarray(mesh.devices).reshape(n_section, n_expert // n_q, n_q, n_dp),
        ("section", "eg", "q", "dp"),
    )
    tok = ("eg", "q", "dp")
    in_specs = (
        P("section", tok, None),
        P("section", None),
        P("section", "dp", ("eg", "q")),
        P("section", "dp", ("eg", "q")),
        P("section", "dp", ("eg", "q")),
        P("section", None, tok, None),
        P("section", None, tok, None),
    )
    out_specs = P("section", tok, None)
    return jax.shard_map(
        on_device, mesh=inner, in_specs=in_specs, out_specs=out_specs, check_vma=False
    )
```

```python
from functools import partial

import jax
import jax.numpy as jnp
import numpy as np
from jax import lax
from jax.sharding import Mesh
from jax.sharding import PartitionSpec as P

ALL = ("eg", "q", "dp")


def passed_along(array, axis, by):
    length = lax.axis_size(axis)
    return lax.ppermute(array, axis, [(i, (i + by) % length) for i in range(length)])


def route(stream, gain_row, routes, experts, capacity):
    tok_rows, model_width = stream.shape
    fan_out = routes.shape[1]
    widened = stream.astype(jnp.float32)
    inv_rms = lax.rsqrt(jnp.mean(widened * widened, axis=1, keepdims=True) + 1e-06)
    normed = (widened * inv_rms * gain_row[None, :]).astype(jnp.bfloat16)
    flat_ids = routes.reshape(-1)
    count_all = flat_ids.shape[0]
    chosen = (flat_ids[:, None] == jnp.arange(experts, dtype=jnp.int32)[None, :]).astype(
        jnp.float32
    )
    triangle = (jnp.arange(count_all)[:, None] >= jnp.arange(count_all)[None, :]).astype(
        jnp.float32
    )
    running = jnp.dot(triangle, chosen, preferred_element_type=jnp.float32)
    slot_of = jnp.sum(chosen * (running - 1.0), axis=1).astype(jnp.int32)
    target = flat_ids * capacity + slot_of
    placing = jnp.arange(experts * capacity, dtype=jnp.int32)[:, None] == target[None, :]
    placing = (
        placing.reshape(experts * capacity, tok_rows, fan_out).any(axis=2).astype(jnp.bfloat16)
    )
    outgoing = jnp.dot(placing, normed, preferred_element_type=jnp.float32).astype(jnp.bfloat16)
    return widened, outgoing.reshape(experts, capacity, model_width), target


def moe_layer(stream, gain_row, gate_w, up_w, down_mine, routes, mixing):
    experts = lax.axis_size("eg")
    blocks = lax.axis_size("q")
    halves = lax.axis_size("dp")
    tok_rows, model_width = stream.shape
    fan_out = routes.shape[1]
    capacity = min(tok_rows, max(2, 5 * tok_rows * fan_out // (4 * experts)))
    half = model_width // halves
    widened, outgoing, target = route(stream, gain_row, routes, experts, capacity)
    lanes = 128
    tiles = half // lanes
    send = outgoing.reshape(experts, capacity, halves, tiles, lanes).transpose(0, 2, 1, 3, 4)
    send = send.reshape(experts * halves, capacity * tiles, lanes)
    arrived = lax.all_to_all(send, ("eg", "dp"), split_axis=0, concat_axis=0, tiled=True)
    arrived = arrived.reshape(experts * halves, capacity, half).transpose(1, 0, 2)
    arrived = lax.all_gather(arrived, "q", axis=1, tiled=True)
    sources = blocks * experts * halves
    rows = arrived.reshape(capacity * sources, half)
    units = gate_w.shape[1]
    both_w = jnp.concatenate([gate_w, up_w], axis=1)
    gate_up = jnp.dot(rows, both_w, preferred_element_type=jnp.float32)
    mine = gate_up.reshape(rows.shape[0], 2, units).transpose(1, 0, 2)
    both = mine + passed_along(mine.astype(jnp.bfloat16), "dp", 1).astype(jnp.float32)
    hidden = (jax.nn.silu(both[0]) * both[1]).astype(jnp.bfloat16)
    hidden_all = lax.all_gather(hidden, "q", axis=1, tiled=True)
    out = lax.dot_general(
        hidden_all, down_mine, (((1,), (1,)), ((), ())), preferred_element_type=jnp.float32
    ).astype(jnp.bfloat16)
    piece = out.shape[1]
    out = out.reshape(capacity, blocks, experts, halves, piece).transpose(2, 1, 3, 0, 4)
    back = lax.all_to_all(
        out.reshape(sources, 2, capacity * piece // 2), ALL, split_axis=0, concat_axis=0, tiled=True
    )
    back = back.reshape(experts, blocks, halves, capacity, piece).transpose(0, 3, 2, 1, 4)
    expert_out = back.reshape(experts * capacity, model_width)
    picked = jnp.take(expert_out, target, axis=0)
    picked = picked.reshape(tok_rows, fan_out, model_width)
    mixed_sum = jnp.sum(mixing[:, :, None] * picked.astype(jnp.float32), axis=1)
    return (widened + mixed_sum).astype(jnp.bfloat16)


def on_device(blocks, gains, w_gate, w_up, w_down, expert_ids, combine):
    stream = blocks[0]
    turns = expert_ids.shape[1]
    n_blocks = lax.axis_size("q")
    down_local = w_down[0]
    half, width = down_local.shape
    piece = half // n_blocks
    down_mine = lax.all_to_all(
        down_local.reshape(n_blocks, piece, width), "q", split_axis=0, concat_axis=0, tiled=True
    )
    down_mine = down_mine.transpose(1, 0, 2).reshape(piece, n_blocks * width)
    for layer_turn in range(turns):
        if layer_turn > 0:
            stream = passed_along(stream, "section", 1)
        stream = moe_layer(
            stream,
            gains[0],
            w_gate[0],
            w_up[0],
            down_mine,
            expert_ids[0, layer_turn],
            combine[0, layer_turn],
        )
    return stream[None]


def solution(mesh):
    n_section, n_expert, n_dp = (mesh.shape[a] for a in ("section", "expert", "dp"))
    n_q = n_expert // 4
    inner = Mesh(
        np.asarray(mesh.devices).reshape(n_section, n_expert // n_q, n_q, n_dp),
        ("section", "eg", "q", "dp"),
    )
    tok = ("eg", "q", "dp")
    in_specs = (
        P("section", tok, None),
        P("section", None),
        P("section", "dp", ("eg", "q")),
        P("section", "dp", ("eg", "q")),
        P("section", "dp", ("eg", "q")),
        P("section", None, tok, None),
        P("section", None, tok, None),
    )
    out_specs = P("section", tok, None)
    return jax.shard_map(
        on_device, mesh=inner, in_specs=in_specs, out_specs=out_specs, check_vma=False
    )
```
